128 devices in a mesh: row: 16 (over y, x_hi, core), col: 8 (over x_lo, z).
Axes of the slice: x: 4 (x_hi: 2, x_lo: 2; x = x_hi * 2 + x_lo), y: 4, z: 4, core: 2. Of those that a mesh axis runs over, the one named last changes fastest.
Arguments:
- matrix: float32 [24576, 4, 3072], P('row', None, 'col'), may hold values from -60 to 60, as said below
Outputs:
- factored: float32 [24576, 4, 3072], P('row', None, 'col')
- r_rows: float32 [2, 384, 4, 3072], P(None, None, None, 'col')
The draws below stay inside these ranges and needn't reach their ends.
Inputs may be any that keep to these rules, and one draw needn't show every extreme that they name: `matrix`: dense real entries with column scales that differ from column to column.
All inputs are finite; a program needn't handle non-finite values.
Results may differ from the reference program's by a relative error of at most 0.00017.
Values sent between devices are 32-bit elements; how exact they have to be, the bound alone decides.
No kernel may reach another device: no remote copies, remote signals or barrier semaphores. Data moves between devices by JAX's collectives and lax.ppermute only.
A program may use at most 128 MiB of HBM per device.

```python
import jax
import jax.numpy as jnp
from jax import lax

B = 384
PANELS_DEV = 4
STEPS = 2
ROWS = 24576
SPAN = 3072
N_COL = 8


def draw_matrix(key, part):
    key_entries = jax.random.fold_in(key, 11)
    key_cols = jax.random.fold_in(key, 12)
    col_scale = jnp.exp(jax.random.uniform(key_cols, (1, PANELS_DEV, SPAN), jnp.float32, jnp.log(0.3), jnp.log(3.0)))
    entries = jax.random.truncated_normal(key_entries, -6.0, 6.0, (ROWS, PANELS_DEV, SPAN), jnp.float32)
    values = entries * col_scale
    return values.astype(jnp.float32)


def setup_inputs(seed: int = 0) -> dict:
    streams_of = jax.random.split(jax.random.key(seed), 2)
    return {
        "matrix": draw_matrix(jax.random.fold_in(streams_of[1], 71), 0),
    }


def reference(matrix):
    highest = lax.Precision.HIGHEST
    count = PANELS_DEV * N_COL
    blocks = matrix.reshape(ROWS, count, B)
    ident = jnp.eye(B, dtype=jnp.float32)
    glob = jnp.arange(count)
    rows_out = []
    for k in range(STEPS):
        panel = blocks[:, k, :]
        gram = jnp.dot(panel.T.astype(jnp.float32), panel.astype(jnp.float32), precision=highest, preferred_element_type=jnp.float32)
        lower = jnp.linalg.cholesky(gram)
        inverse = lax.linalg.triangular_solve(lower, ident, left_side=True, lower=True)
        basis = jnp.dot(panel.astype(jnp.float32), inverse.T.astype(jnp.float32), precision=highest, preferred_element_type=jnp.float32)
        proj = jnp.einsum('mb,mgt->bgt', basis, blocks, precision=highest)
        kept = jnp.where((glob > k)[None, :, None], proj, jnp.float32(0.0))
        blocks = blocks - jnp.einsum('mb,bgt->mgt', basis, kept, precision=highest)
        blocks = jnp.where((glob == k)[None, :, None], basis[:, None, :], blocks)
        rows_out.append(jnp.where((glob == k)[None, :, None], lower.T[:, None, :], kept))
    factored = blocks.reshape(ROWS, PANELS_DEV, SPAN)
    r_rows = jnp.stack(rows_out).reshape(STEPS, B, PANELS_DEV, SPAN)
    return (factored, r_rows)
```

```python
import jax
import jax.numpy as jnp
from jax import lax
from jax.sharding import PartitionSpec as P

STEPS = 2


def shards(matrix):
    highest = lax.Precision.HIGHEST
    column = lax.axis_index("col")
    ncol = lax.axis_size("col")
    count = matrix.shape[1]
    width = matrix.shape[2]
    glob = jnp.arange(count, dtype=jnp.int32) * ncol + column
    ident = jnp.eye(width, dtype=jnp.float32)
    own = matrix[:, 0, :]
    zero = jnp.zeros_like(own)
    both = lax.psum(
        jnp.concatenate(
            [jnp.where(column == 0, own, zero), jnp.where(column == 1, own, zero)], axis=1
        ),
        "col",
    )
    gram_part = jnp.dot(both.T, both, precision=highest, preferred_element_type=jnp.float32)
    cross_part = jnp.einsum("mb,mjt->bjt", both, matrix, precision=highest)
    gram, cross = lax.psum((gram_part, cross_part), "row")
    g00 = gram[:width, :width]
    g10 = gram[width:, :width]
    g11 = gram[width:, width:]
    lower0 = jnp.linalg.cholesky(g00)
    inv0 = lax.linalg.triangular_solve(lower0, ident, left_side=True, lower=True)
    xmat = jnp.dot(g10, inv0.T, precision=highest, preferred_element_type=jnp.float32)
    schur = g11 - jnp.dot(xmat, xmat.T, precision=highest, preferred_element_type=jnp.float32)
    lower1 = jnp.linalg.cholesky(schur)
    inv1 = lax.linalg.triangular_solve(lower1, ident, left_side=True, lower=True)
    proj0 = jnp.einsum("ab,bjt->ajt", inv0, cross[:width], precision=highest)
    rest1 = cross[width:] - jnp.einsum("ab,bjt->ajt", xmat, proj0, precision=highest)
    proj1 = jnp.einsum("ab,bjt->ajt", inv1, rest1, precision=highest)
    panel0 = both[:, :width]
    panel1 = both[:, width:]
    basis0 = jnp.dot(panel0, inv0.T, precision=highest, preferred_element_type=jnp.float32)
    resid1 = panel1 - jnp.dot(basis0, xmat.T, precision=highest, preferred_element_type=jnp.float32)
    basis1 = jnp.dot(resid1, inv1.T, precision=highest, preferred_element_type=jnp.float32)
    kept0 = jnp.where((glob > 0)[None, :, None], proj0, jnp.float32(0.0))
    kept1 = jnp.where((glob > 1)[None, :, None], proj1, jnp.float32(0.0))
    basis = jnp.concatenate([basis0, basis1], axis=1)
    kept = jnp.concatenate([kept0, kept1], axis=0)
    blocks = matrix - jnp.einsum("mb,bjt->mjt", basis, kept, precision=highest)
    blocks = jnp.where((glob == 0)[None, :, None], basis0[:, None, :], blocks)
    blocks = jnp.where((glob == 1)[None, :, None], basis1[:, None, :], blocks)
    row0 = jnp.where((glob == 0)[None, :, None], lower0.T[:, None, :], kept0)
    row1 = jnp.where((glob == 1)[None, :, None], lower1.T[:, None, :], kept1)
    return (blocks, jnp.stack([row0, row1]))


def solution(mesh):
    return jax.shard_map(
        shards,
        mesh=mesh,
        in_specs=(P("row", None, "col"),),
        out_specs=(P("row", None, "col"), P(None, None, None, "col")),
        check_vma=False,
    )
```

```python
import jax
import jax.numpy as jnp
from jax import lax
from jax.sharding import PartitionSpec as P
from jax.experimental import pallas as pl
from jax.experimental.pallas import tpu as pltpu

STEPS = 2

TILE = 128
GROUP = 8


def _chol_inv_kernel(a_ref, u_ref, m_ref, w_ref):
    n = a_ref.shape[0]
    w_ref[...] = a_ref[...]
    u_ref[...] = jnp.zeros_like(u_ref)
    rows = lax.broadcasted_iota(jnp.int32, (n, n), 0)
    cols = lax.broadcasted_iota(jnp.int32, (n, n), 1)
    m_ref[...] = jnp.where(rows == cols, 1.0, 0.0).astype(jnp.float32)
    for b in range(n // TILE):
        lo = b * TILE
        span = n - lo
        done = lo + TILE

        def group(q, carry, lo=lo, span=span, done=done):
            base = pl.multiple_of(lo + q * GROUP, GROUP)
            sub = lax.broadcasted_iota(jnp.int32, (GROUP, 1), 0)
            lane = lax.broadcasted_iota(jnp.int32, (1, span), 1)
            tlane = lax.broadcasted_iota(jnp.int32, (span, TILE), 1)
            rid = lax.broadcasted_iota(jnp.int32, (span, 1), 0)
            for r in range(GROUP):
                kk = q * GROUP + r
                a_row = w_ref[pl.ds(base, GROUP), pl.ds(lo, span)][r:r + 1, :]
                pivot = jnp.sum(jnp.where(lane == kk, a_row, 0.0), axis=1, keepdims=True)
                scale = 1.0 / jnp.sqrt(pivot)
                u = jnp.where(lane >= kk, a_row * scale, 0.0)
                u8 = u_ref[pl.ds(base, GROUP), pl.ds(lo, span)]
                u_ref[pl.ds(base, GROUP), pl.ds(lo, span)] = jnp.where(sub == r, u, u8)
                m8 = m_ref[pl.ds(base, GROUP), pl.ds(0, done)]
                m_row = m8[r:r + 1, :] * scale
                m_ref[pl.ds(base, GROUP), pl.ds(0, done)] = jnp.where(sub == r, m_row, m8)
                tile = w_ref[pl.ds(lo, span), pl.ds(lo, TILE)]
                ucol = jnp.sum(jnp.where(tlane == kk, tile, 0.0), axis=1, keepdims=True) * scale
                ucol = jnp.where(rid > kk, ucol, 0.0)
                w_ref[pl.ds(lo, span), pl.ds(lo, span)] = w_ref[pl.ds(lo, span), pl.ds(lo, span)] - ucol * u
                m_ref[pl.ds(lo, span), pl.ds(0, done)] = m_ref[pl.ds(lo, span), pl.ds(0, done)] - ucol * m_row
            return carry

        lax.fori_loop(0, TILE // GROUP, group, 0)


def chol_inv(a):
    n = a.shape[0]
    return pl.pallas_call(
        _chol_inv_kernel,
        out_shape=(jax.ShapeDtypeStruct((n, n), jnp.float32), jax.ShapeDtypeStruct((n, n), jnp.float32)),
        scratch_shapes=[pltpu.VMEM((n, n), jnp.float32)],
        cost_estimate=pl.CostEstimate(flops=2 * n * n * n, bytes_accessed=3 * n * n * 4, transcendentals=n),
    )(a)


def symmetric(a):
    return (a + a.T) * jnp.float32(0.5)


def shards(matrix):
    highest = lax.Precision.HIGHEST
    column = lax.axis_index("col")
    ncol = lax.axis_size("col")
    count = matrix.shape[1]
    width = matrix.shape[2]
    glob = jnp.arange(count, dtype=jnp.int32) * ncol + column
    own = matrix[:, 0, :]
    zero = jnp.zeros_like(own)
    both = lax.psum(
        jnp.concatenate(
            [jnp.where(column == 0, own, zero), jnp.where(column == 1, own, zero)], axis=1
        ),
        "col",
    )
    gram_part = jnp.dot(both.T, both, precision=highest, preferred_element_type=jnp.float32)
    cross_part = jnp.einsum("mb,mjt->bjt", both, matrix, precision=highest)
    gram, cross = lax.psum((gram_part, cross_part), "row")
    g00 = gram[:width, :width]
    g10 = gram[width:, :width]
    g11 = gram[width:, width:]
    upper0, inv0 = chol_inv(symmetric(g00))
    xmat = jnp.dot(g10, inv0.T, precision=highest, preferred_element_type=jnp.float32)
    schur = g11 - jnp.dot(xmat, xmat.T, precision=highest, preferred_element_type=jnp.float32)
    upper1, inv1 = chol_inv(symmetric(schur))
    proj0 = jnp.einsum("ab,bjt->ajt", inv0, cross[:width], precision=highest)
    rest1 = cross[width:] - jnp.einsum("ab,bjt->ajt", xmat, proj0, precision=highest)
    proj1 = jnp.einsum("ab,bjt->ajt", inv1, rest1, precision=highest)
    panel0 = both[:, :width]
    panel1 = both[:, width:]
    basis0 = jnp.dot(panel0, inv0.T, precision=highest, preferred_element_type=jnp.float32)
    resid1 = panel1 - jnp.dot(basis0, xmat.T, precision=highest, preferred_element_type=jnp.float32)
    basis1 = jnp.dot(resid1, inv1.T, precision=highest, preferred_element_type=jnp.float32)
    kept0 = jnp.where((glob > 0)[None, :, None], proj0, jnp.float32(0.0))
    kept1 = jnp.where((glob > 1)[None, :, None], proj1, jnp.float32(0.0))
    basis = jnp.concatenate([basis0, basis1], axis=1)
    kept = jnp.concatenate([kept0, kept1], axis=0)
    blocks = matrix - jnp.einsum("mb,bjt->mjt", basis, kept, precision=highest)
    blocks = jnp.where((glob == 0)[None, :, None], basis0[:, None, :], blocks)
    blocks = jnp.where((glob == 1)[None, :, None], basis1[:, None, :], blocks)
    row0 = jnp.where((glob == 0)[None, :, None], upper0[:, None, :], kept0)
    row1 = jnp.where((glob == 1)[None, :, None], upper1[:, None, :], kept1)
    return (blocks, jnp.stack([row0, row1]))


def solution(mesh):
    return jax.shard_map(
        shards,
        mesh=mesh,
        in_specs=(P("row", None, "col"),),
        out_specs=(P("row", None, "col"), P(None, None, None, "col")),
        check_vma=False,
    )
```

```python
import jax
import jax.numpy as jnp
from jax import lax
from jax.sharding import PartitionSpec as P
from jax.experimental import pallas as pl
from jax.experimental.pallas import tpu as pltpu

STEPS = 2

TILE = 128
GROUP = 8


def _chol_inv_kernel(a_ref, u_ref, m_ref, w_ref):
    n = a_ref.shape[0]
    w_ref[...] = a_ref[...]
    u_ref[...] = jnp.zeros_like(u_ref)
    rows = lax.broadcasted_iota(jnp.int32, (n, n), 0)
    cols = lax.broadcasted_iota(jnp.int32, (n, n), 1)
    m_ref[...] = jnp.where(rows == cols, 1.0, 0.0).astype(jnp.float32)
    for b in range(n // TILE):
        lo = b * TILE
        span = n - lo
        done = lo + TILE

        def group(q, carry, lo=lo, span=span, done=done):
            base = pl.multiple_of(lo + q * GROUP, GROUP)
            sub = lax.broadcasted_iota(jnp.int32, (GROUP, 1), 0)
            lane = lax.broadcasted_iota(jnp.int32, (1, span), 1)
            tlane = lax.broadcasted_iota(jnp.int32, (span, TILE), 1)
            rid = lax.broadcasted_iota(jnp.int32, (span, 1), 0)
            for r in range(GROUP):
                kk = q * GROUP + r
                a_row = w_ref[pl.ds(base, GROUP), pl.ds(lo, span)][r:r + 1, :]
                pivot = jnp.sum(jnp.where(lane == kk, a_row, 0.0), axis=1, keepdims=True)
                scale = 1.0 / jnp.sqrt(pivot)
                u = jnp.where(lane >= kk, a_row * scale, 0.0)
                u8 = u_ref[pl.ds(base, GROUP), pl.ds(lo, span)]
                u_ref[pl.ds(base, GROUP), pl.ds(lo, span)] = jnp.where(sub == r, u, u8)
                m8 = m_ref[pl.ds(base, GROUP), pl.ds(0, done)]
                m_row = m8[r:r + 1, :] * scale
                m_ref[pl.ds(base, GROUP), pl.ds(0, done)] = jnp.where(sub == r, m_row, m8)
                tile = w_ref[pl.ds(lo, span), pl.ds(lo, TILE)]
                ucol = jnp.sum(jnp.where(tlane == kk, tile, 0.0), axis=1, keepdims=True) * scale
                ucol = jnp.where(rid > kk, ucol, 0.0)
                w_ref[pl.ds(lo, span), pl.ds(lo, span)] = w_ref[pl.ds(lo, span), pl.ds(lo, span)] - ucol * u
                m_ref[pl.ds(lo, span), pl.ds(0, done)] = m_ref[pl.ds(lo, span), pl.ds(0, done)] - ucol * m_row
            return carry

        lax.fori_loop(0, TILE // GROUP, group, 0)


def chol_inv(a):
    n = a.shape[0]
    return pl.pallas_call(
        _chol_inv_kernel,
        out_shape=(jax.ShapeDtypeStruct((n, n), jnp.float32), jax.ShapeDtypeStruct((n, n), jnp.float32)),
        scratch_shapes=[pltpu.VMEM((n, n), jnp.float32)],
        cost_estimate=pl.CostEstimate(flops=2 * n * n * n, bytes_accessed=3 * n * n * 4, transcendentals=n),
    )(a)


def symmetric(a):
    return (a + a.T) * jnp.float32(0.5)


def shards(matrix):
    highest = lax.Precision.HIGHEST
    column = lax.axis_index("col")
    ncol = lax.axis_size("col")
    count = matrix.shape[1]
    width = matrix.shape[2]
    glob = jnp.arange(count, dtype=jnp.int32) * ncol + column
    own = matrix[:, 0, :]
    zero = jnp.zeros_like(own)
    both = lax.psum(
        jnp.concatenate(
            [jnp.where(column == 0, own, zero), jnp.where(column == 1, own, zero)], axis=1
        ),
        "col",
    )
    gram_part = jnp.dot(both.T, both, precision=highest, preferred_element_type=jnp.float32)
    cross_part = jnp.einsum("mb,mjt->bjt", both, matrix, precision=lax.Precision.HIGH)
    gram, cross = lax.psum((gram_part, cross_part), "row")
    g00 = gram[:width, :width]
    g10 = gram[width:, :width]
    g11 = gram[width:, width:]
    upper0, inv0 = chol_inv(symmetric(g00))
    xmat = jnp.dot(g10, inv0.T, precision=highest, preferred_element_type=jnp.float32)
    schur = g11 - jnp.dot(xmat, xmat.T, precision=highest, preferred_element_type=jnp.float32)
    upper1, inv1 = chol_inv(symmetric(schur))
    proj0 = jnp.einsum("ab,bjt->ajt", inv0, cross[:width], precision=highest)
    rest1 = cross[width:] - jnp.einsum("ab,bjt->ajt", xmat, proj0, precision=highest)
    proj1 = jnp.einsum("ab,bjt->ajt", inv1, rest1, precision=highest)
    panel0 = both[:, :width]
    panel1 = both[:, width:]
    basis0 = jnp.dot(panel0, inv0.T, precision=highest, preferred_element_type=jnp.float32)
    resid1 = panel1 - jnp.dot(basis0, xmat.T, precision=highest, preferred_element_type=jnp.float32)
    basis1 = jnp.dot(resid1, inv1.T, precision=highest, preferred_element_type=jnp.float32)
    kept0 = jnp.where((glob > 0)[None, :, None], proj0, jnp.float32(0.0))
    kept1 = jnp.where((glob > 1)[None, :, None], proj1, jnp.float32(0.0))
    basis = jnp.concatenate([basis0, basis1], axis=1)
    kept = jnp.concatenate([kept0, kept1], axis=0)
    blocks = matrix - jnp.einsum("mb,bjt->mjt", basis, kept, precision=lax.Precision.HIGH)
    blocks = jnp.where((glob == 0)[None, :, None], basis0[:, None, :], blocks)
    blocks = jnp.where((glob == 1)[None, :, None], basis1[:, None, :], blocks)
    row0 = jnp.where((glob == 0)[None, :, None], upper0[:, None, :], kept0)
    row1 = jnp.where((glob == 1)[None, :, None], upper1[:, None, :], kept1)
    return (blocks, jnp.stack([row0, row1]))


def solution(mesh):
    return jax.shard_map(
        shards,
        mesh=mesh,
        in_specs=(P("row", None, "col"),),
        out_specs=(P("row", None, "col"), P(None, None, None, "col")),
        check_vma=False,
    )
```

```python
import jax
import jax.numpy as jnp
from jax import lax
from jax.sharding import PartitionSpec as P
from jax.experimental import pallas as pl
from jax.experimental.pallas import tpu as pltpu

STEPS = 2

TILE = 128
GROUP = 8


def _mm(a, b):
    return jnp.dot(a, b, precision=lax.Precision.HIGHEST, preferred_element_type=jnp.float32)


def _chol_inv_kernel(a_ref, u_ref, m_ref, w_ref, t_ref, d_ref, e_ref):
    n = a_ref.shape[0]
    nb = n // TILE
    w_ref[...] = a_ref[...]
    u_ref[...] = jnp.zeros_like(u_ref)
    m_ref[...] = jnp.zeros_like(m_ref)
    rows = lax.broadcasted_iota(jnp.int32, (TILE, TILE), 0)
    cols = lax.broadcasted_iota(jnp.int32, (TILE, TILE), 1)
    eye = jnp.where(rows == cols, 1.0, 0.0).astype(jnp.float32)
    sub = lax.broadcasted_iota(jnp.int32, (GROUP, 1), 0)
    lane = lax.broadcasted_iota(jnp.int32, (1, TILE), 1)
    rid = lax.broadcasted_iota(jnp.int32, (TILE, 1), 0)
    for b in range(nb):
        lo = b * TILE
        hi = lo + TILE
        t_ref[...] = w_ref[lo:hi, lo:hi]
        d_ref[...] = eye
        e_ref[...] = jnp.zeros_like(e_ref)

        def group(q, carry):
            base = pl.multiple_of(q * GROUP, GROUP)
            for r in range(GROUP):
                kk = q * GROUP + r
                a_row = t_ref[pl.ds(base, GROUP), :][r:r + 1, :]
                pivot = jnp.sum(jnp.where(lane == kk, a_row, 0.0), axis=1, keepdims=True)
                scale = 1.0 / jnp.sqrt(pivot)
                u = jnp.where(lane >= kk, a_row * scale, 0.0)
                u8 = e_ref[pl.ds(base, GROUP), :]
                e_ref[pl.ds(base, GROUP), :] = jnp.where(sub == r, u, u8)
                m8 = d_ref[pl.ds(base, GROUP), :]
                m_row = m8[r:r + 1, :] * scale
                d_ref[pl.ds(base, GROUP), :] = jnp.where(sub == r, m_row, m8)
                tile = t_ref[...]
                ucol = jnp.sum(jnp.where(cols == kk, tile, 0.0), axis=1, keepdims=True) * scale
                ucol = jnp.where(rid > kk, ucol, 0.0)
                t_ref[...] = tile - ucol * u
                d_ref[...] = d_ref[...] - ucol * m_row
            return carry

        lax.fori_loop(0, TILE // GROUP, group, 0)
        u_ref[lo:hi, lo:hi] = e_ref[...]
        m_ref[lo:hi, lo:hi] = d_ref[...]
        if b + 1 < nb:
            panel = _mm(d_ref[...], w_ref[lo:hi, hi:n])
            u_ref[lo:hi, hi:n] = panel
            w_ref[hi:n, hi:n] = w_ref[hi:n, hi:n] - _mm(panel.T, panel)
    for i in range(1, nb):
        di = m_ref[i * TILE:(i + 1) * TILE, i * TILE:(i + 1) * TILE]
        for j in range(i - 1, -1, -1):
            acc = jnp.zeros((TILE, TILE), jnp.float32)
            for k in range(j, i):
                low_ik = u_ref[k * TILE:(k + 1) * TILE, i * TILE:(i + 1) * TILE].T
                acc = acc + _mm(low_ik, m_ref[k * TILE:(k + 1) * TILE, j * TILE:(j + 1) * TILE])
            m_ref[i * TILE:(i + 1) * TILE, j * TILE:(j + 1) * TILE] = -_mm(di, acc)


def chol_inv(a):
    n = a.shape[0]
    return pl.pallas_call(
        _chol_inv_kernel,
        out_shape=(jax.ShapeDtypeStruct((n, n), jnp.float32), jax.ShapeDtypeStruct((n, n), jnp.float32)),
        scratch_shapes=[
            pltpu.VMEM((n, n), jnp.float32),
            pltpu.VMEM((TILE, TILE), jnp.float32),
            pltpu.VMEM((TILE, TILE), jnp.float32),
            pltpu.VMEM((TILE, TILE), jnp.float32),
        ],
        cost_estimate=pl.CostEstimate(flops=2 * n * n * n, bytes_accessed=3 * n * n * 4, transcendentals=n),
    )(a)


def symmetric(a):
    return (a + a.T) * jnp.float32(0.5)


def shards(matrix):
    highest = lax.Precision.HIGHEST
    column = lax.axis_index("col")
    ncol = lax.axis_size("col")
    count = matrix.shape[1]
    width = matrix.shape[2]
    glob = jnp.arange(count, dtype=jnp.int32) * ncol + column
    own = matrix[:, 0, :]
    zero = jnp.zeros_like(own)
    both = lax.psum(
        jnp.concatenate(
            [jnp.where(column == 0, own, zero), jnp.where(column == 1, own, zero)], axis=1
        ),
        "col",
    )
    gram_part = jnp.dot(both.T, both, precision=highest, preferred_element_type=jnp.float32)
    cross_part = jnp.einsum("mb,mjt->bjt", both, matrix, precision=lax.Precision.HIGH)
    gram, cross = lax.psum((gram_part, cross_part), "row")
    g00 = gram[:width, :width]
    g10 = gram[width:, :width]
    g11 = gram[width:, width:]
    upper0, inv0 = chol_inv(symmetric(g00))
    xmat = jnp.dot(g10, inv0.T, precision=highest, preferred_element_type=jnp.float32)
    schur = g11 - jnp.dot(xmat, xmat.T, precision=highest, preferred_element_type=jnp.float32)
    upper1, inv1 = chol_inv(symmetric(schur))
    proj0 = jnp.einsum("ab,bjt->ajt", inv0, cross[:width], precision=highest)
    rest1 = cross[width:] - jnp.einsum("ab,bjt->ajt", xmat, proj0, precision=highest)
    proj1 = jnp.einsum("ab,bjt->ajt", inv1, rest1, precision=highest)
    panel0 = both[:, :width]
    panel1 = both[:, width:]
    basis0 = jnp.dot(panel0, inv0.T, precision=highest, preferred_element_type=jnp.float32)
    resid1 = panel1 - jnp.dot(basis0, xmat.T, precision=highest, preferred_element_type=jnp.float32)
    basis1 = jnp.dot(resid1, inv1.T, precision=highest, preferred_element_type=jnp.float32)
    kept0 = jnp.where((glob > 0)[None, :, None], proj0, jnp.float32(0.0))
    kept1 = jnp.where((glob > 1)[None, :, None], proj1, jnp.float32(0.0))
    basis = jnp.concatenate([basis0, basis1], axis=1)
    kept = jnp.concatenate([kept0, kept1], axis=0)
    blocks = matrix - jnp.einsum("mb,bjt->mjt", basis, kept, precision=lax.Precision.HIGH)
    blocks = jnp.where((glob == 0)[None, :, None], basis0[:, None, :], blocks)
    blocks = jnp.where((glob == 1)[None, :, None], basis1[:, None, :], blocks)
    row0 = jnp.where((glob == 0)[None, :, None], upper0[:, None, :], kept0)
    row1 = jnp.where((glob == 1)[None, :, None], upper1[:, None, :], kept1)
    return (blocks, jnp.stack([row0, row1]))


def solution(mesh):
    return jax.shard_map(
        shards,
        mesh=mesh,
        in_specs=(P("row", None, "col"),),
        out_specs=(P("row", None, "col"), P(None, None, None, "col")),
        check_vma=False,
    )
```

```python
import jax
import jax.numpy as jnp
from jax import lax
from jax.sharding import PartitionSpec as P
from jax.experimental import pallas as pl
from jax.experimental.pallas import tpu as pltpu

STEPS = 2

TILE = 128
GROUP = 8


def _mm(a, b):
    return jnp.dot(a, b, precision=lax.Precision.HIGHEST, preferred_element_type=jnp.float32)


def _chol_inv_kernel(a_ref, u_ref, m_ref, w_ref, t_ref, d_ref, e_ref):
    n = a_ref.shape[0]
    nb = n // TILE
    w_ref[...] = a_ref[...]
    u_ref[...] = jnp.zeros_like(u_ref)
    m_ref[...] = jnp.zeros_like(m_ref)
    rows = lax.broadcasted_iota(jnp.int32, (TILE, TILE), 0)
    cols = lax.broadcasted_iota(jnp.int32, (TILE, TILE), 1)
    eye = jnp.where(rows == cols, 1.0, 0.0).astype(jnp.float32)
    sub = lax.broadcasted_iota(jnp.int32, (GROUP, 1), 0)
    lane = lax.broadcasted_iota(jnp.int32, (1, TILE), 1)
    rid = lax.broadcasted_iota(jnp.int32, (TILE, 1), 0)
    for b in range(nb):
        lo = b * TILE
        hi = lo + TILE
        t_ref[...] = w_ref[lo:hi, lo:hi]
        d_ref[...] = eye
        e_ref[...] = jnp.zeros_like(e_ref)

        def group(q, carry):
            base = pl.multiple_of(q * GROUP, GROUP)
            for r in range(GROUP):
                kk = q * GROUP + r
                a_row = t_ref[pl.ds(base, GROUP), :][r:r + 1, :]
                pivot = jnp.sum(jnp.where(lane == kk, a_row, 0.0), axis=1, keepdims=True)
                scale = 1.0 / jnp.sqrt(pivot)
                u = jnp.where(lane >= kk, a_row * scale, 0.0)
                u8 = e_ref[pl.ds(base, GROUP), :]
                e_ref[pl.ds(base, GROUP), :] = jnp.where(sub == r, u, u8)
                m8 = d_ref[pl.ds(base, GROUP), :]
                m_row = m8[r:r + 1, :] * scale
                d_ref[pl.ds(base, GROUP), :] = jnp.where(sub == r, m_row, m8)
                tile = t_ref[...]
                ucol = jnp.sum(jnp.where(cols == kk, tile, 0.0), axis=1, keepdims=True) * scale
                ucol = jnp.where(rid > kk, ucol, 0.0)
                t_ref[...] = tile - ucol * u
                d_ref[...] = d_ref[...] - ucol * m_row
            return carry

        lax.fori_loop(0, TILE // GROUP, group, 0)
        u_ref[lo:hi, lo:hi] = e_ref[...]
        m_ref[lo:hi, lo:hi] = d_ref[...]
        if b + 1 < nb:
            panel = _mm(d_ref[...], w_ref[lo:hi, hi:n])
            u_ref[lo:hi, hi:n] = panel
            w_ref[hi:n, hi:n] = w_ref[hi:n, hi:n] - _mm(panel.T, panel)
    for i in range(1, nb):
        di = m_ref[i * TILE:(i + 1) * TILE, i * TILE:(i + 1) * TILE]
        for j in range(i - 1, -1, -1):
            acc = jnp.zeros((TILE, TILE), jnp.float32)
            for k in range(j, i):
                low_ik = u_ref[k * TILE:(k + 1) * TILE, i * TILE:(i + 1) * TILE].T
                acc = acc + _mm(low_ik, m_ref[k * TILE:(k + 1) * TILE, j * TILE:(j + 1) * TILE])
            m_ref[i * TILE:(i + 1) * TILE, j * TILE:(j + 1) * TILE] = -_mm(di, acc)


def chol_inv(a):
    n = a.shape[0]
    return pl.pallas_call(
        _chol_inv_kernel,
        out_shape=(jax.ShapeDtypeStruct((n, n), jnp.float32), jax.ShapeDtypeStruct((n, n), jnp.float32)),
        scratch_shapes=[
            pltpu.VMEM((n, n), jnp.float32),
            pltpu.VMEM((TILE, TILE), jnp.float32),
            pltpu.VMEM((TILE, TILE), jnp.float32),
            pltpu.VMEM((TILE, TILE), jnp.float32),
        ],
        cost_estimate=pl.CostEstimate(flops=2 * n * n * n, bytes_accessed=3 * n * n * 4, transcendentals=n),
    )(a)


def symmetric(a):
    return (a + a.T) * jnp.float32(0.5)


def shards(matrix):
    highest = lax.Precision.HIGHEST
    column = lax.axis_index("col")
    ncol = lax.axis_size("col")
    count = matrix.shape[1]
    width = matrix.shape[2]
    glob = jnp.arange(count, dtype=jnp.int32) * ncol + column
    own = matrix[:, 0, :]
    zero = jnp.zeros_like(own)
    panel0, panel1 = lax.psum(
        (jnp.where(column == 0, own, zero), jnp.where(column == 1, own, zero)), "col"
    )
    high = lax.Precision.HIGH
    parts = (
        jnp.dot(panel0.T, panel0, precision=highest, preferred_element_type=jnp.float32),
        jnp.dot(panel1.T, panel0, precision=highest, preferred_element_type=jnp.float32),
        jnp.dot(panel1.T, panel1, precision=highest, preferred_element_type=jnp.float32),
        jnp.einsum("mb,mjt->bjt", panel0, matrix, precision=high),
        jnp.einsum("mb,mjt->bjt", panel1, matrix, precision=high),
    )
    g00, g10, g11, cross0, cross1 = lax.psum(parts, "row")
    upper0, inv0 = chol_inv(symmetric(g00))
    xmat = jnp.dot(g10, inv0.T, precision=highest, preferred_element_type=jnp.float32)
    schur = g11 - jnp.dot(xmat, xmat.T, precision=highest, preferred_element_type=jnp.float32)
    upper1, inv1 = chol_inv(symmetric(schur))
    proj0 = jnp.einsum("ab,bjt->ajt", inv0, cross0, precision=high)
    rest1 = cross1 - jnp.einsum("ab,bjt->ajt", xmat, proj0, precision=high)
    proj1 = jnp.einsum("ab,bjt->ajt", inv1, rest1, precision=high)
    basis0 = jnp.dot(panel0, inv0.T, precision=high, preferred_element_type=jnp.float32)
    resid1 = panel1 - jnp.dot(basis0, xmat.T, precision=high, preferred_element_type=jnp.float32)
    basis1 = jnp.dot(resid1, inv1.T, precision=high, preferred_element_type=jnp.float32)
    kept0 = jnp.where((glob > 0)[None, :, None], proj0, jnp.float32(0.0))
    kept1 = jnp.where((glob > 1)[None, :, None], proj1, jnp.float32(0.0))
    basis = jnp.concatenate([basis0, basis1], axis=1)
    kept = jnp.concatenate([kept0, kept1], axis=0)
    blocks = matrix - jnp.einsum("mb,bjt->mjt", basis, kept, precision=high)
    blocks = jnp.where((glob == 0)[None, :, None], basis0[:, None, :], blocks)
    blocks = jnp.where((glob == 1)[None, :, None], basis1[:, None, :], blocks)
    row0 = jnp.where((glob == 0)[None, :, None], upper0[:, None, :], kept0)
    row1 = jnp.where((glob == 1)[None, :, None], upper1[:, None, :], kept1)
    return (blocks, jnp.stack([row0, row1]))


def solution(mesh):
    return jax.shard_map(
        shards,
        mesh=mesh,
        in_specs=(P("row", None, "col"),),
        out_specs=(P("row", None, "col"), P(None, None, None, "col")),
        check_vma=False,
    )
```

```python
import jax
import jax.numpy as jnp
from jax import lax
from jax.sharding import PartitionSpec as P
from jax.experimental.layout import Layout, with_layout_constraint
from jax.experimental import pallas as pl
from jax.experimental.pallas import tpu as pltpu

STEPS = 2

TILE = 128
GROUP = 8


def _mm(a, b):
    return jnp.dot(a, b, precision=lax.Precision.HIGHEST, preferred_element_type=jnp.float32)


def _chol_inv_kernel(a_ref, u_ref, m_ref, w_ref, t_ref, d_ref, e_ref):
    n = a_ref.shape[0]
    nb = n // TILE
    w_ref[...] = a_ref[...]
    u_ref[...] = jnp.zeros_like(u_ref)
    m_ref[...] = jnp.zeros_like(m_ref)
    rows = lax.broadcasted_iota(jnp.int32, (TILE, TILE), 0)
    cols = lax.broadcasted_iota(jnp.int32, (TILE, TILE), 1)
    eye = jnp.where(rows == cols, 1.0, 0.0).astype(jnp.float32)
    sub = lax.broadcasted_iota(jnp.int32, (GROUP, 1), 0)
    lane = lax.broadcasted_iota(jnp.int32, (1, TILE), 1)
    rid = lax.broadcasted_iota(jnp.int32, (TILE, 1), 0)
    for b in range(nb):
        lo = b * TILE
        hi = lo + TILE
        t_ref[...] = w_ref[lo:hi, lo:hi]
        d_ref[...] = eye
        e_ref[...] = jnp.zeros_like(e_ref)

        def group(q, carry):
            base = pl.multiple_of(q * GROUP, GROUP)
            for r in range(GROUP):
                kk = q * GROUP + r
                a_row = t_ref[pl.ds(base, GROUP), :][r:r + 1, :]
                pivot = jnp.sum(jnp.where(lane == kk, a_row, 0.0), axis=1, keepdims=True)
                scale = 1.0 / jnp.sqrt(pivot)
                u = jnp.where(lane >= kk, a_row * scale, 0.0)
                u8 = e_ref[pl.ds(base, GROUP), :]
                e_ref[pl.ds(base, GROUP), :] = jnp.where(sub == r, u, u8)
                m8 = d_ref[pl.ds(base, GROUP), :]
                m_row = m8[r:r + 1, :] * scale
                d_ref[pl.ds(base, GROUP), :] = jnp.where(sub == r, m_row, m8)
                tile = t_ref[...]
                ucol = jnp.sum(jnp.where(cols == kk, tile, 0.0), axis=1, keepdims=True) * scale
                ucol = jnp.where(rid > kk, ucol, 0.0)
                t_ref[...] = tile - ucol * u
                d_ref[...] = d_ref[...] - ucol * m_row
            return carry

        lax.fori_loop(0, TILE // GROUP, group, 0)
        u_ref[lo:hi, lo:hi] = e_ref[...]
        m_ref[lo:hi, lo:hi] = d_ref[...]
        if b + 1 < nb:
            panel = _mm(d_ref[...], w_ref[lo:hi, hi:n])
            u_ref[lo:hi, hi:n] = panel
            w_ref[hi:n, hi:n] = w_ref[hi:n, hi:n] - _mm(panel.T, panel)
    for i in range(1, nb):
        di = m_ref[i * TILE:(i + 1) * TILE, i * TILE:(i + 1) * TILE]
        for j in range(i - 1, -1, -1):
            acc = jnp.zeros((TILE, TILE), jnp.float32)
            for k in range(j, i):
                low_ik = u_ref[k * TILE:(k + 1) * TILE, i * TILE:(i + 1) * TILE].T
                acc = acc + _mm(low_ik, m_ref[k * TILE:(k + 1) * TILE, j * TILE:(j + 1) * TILE])
            m_ref[i * TILE:(i + 1) * TILE, j * TILE:(j + 1) * TILE] = -_mm(di, acc)


def chol_inv(a):
    n = a.shape[0]
    return pl.pallas_call(
        _chol_inv_kernel,
        out_shape=(jax.ShapeDtypeStruct((n, n), jnp.float32), jax.ShapeDtypeStruct((n, n), jnp.float32)),
        scratch_shapes=[
            pltpu.VMEM((n, n), jnp.float32),
            pltpu.VMEM((TILE, TILE), jnp.float32),
            pltpu.VMEM((TILE, TILE), jnp.float32),
            pltpu.VMEM((TILE, TILE), jnp.float32),
        ],
        cost_estimate=pl.CostEstimate(flops=2 * n * n * n, bytes_accessed=3 * n * n * 4, transcendentals=n),
    )(a)


def symmetric(a):
    return (a + a.T) * jnp.float32(0.5)


def shards(matrix):
    highest = lax.Precision.HIGHEST
    column = lax.axis_index("col")
    ncol = lax.axis_size("col")
    count = matrix.shape[1]
    width = matrix.shape[2]
    glob = jnp.arange(count, dtype=jnp.int32) * ncol + column
    own = matrix[:, 0, :]
    zero = jnp.zeros_like(own)
    panel0, panel1 = lax.psum(
        (jnp.where(column == 0, own, zero), jnp.where(column == 1, own, zero)), "col"
    )
    high = lax.Precision.HIGH
    parts = (
        jnp.dot(panel0.T, panel0, precision=highest, preferred_element_type=jnp.float32),
        jnp.dot(panel1.T, panel0, precision=highest, preferred_element_type=jnp.float32),
        jnp.dot(panel1.T, panel1, precision=highest, preferred_element_type=jnp.float32),
        jnp.einsum("mb,mjt->bjt", panel0, matrix, precision=high),
        jnp.einsum("mb,mjt->bjt", panel1, matrix, precision=high),
    )
    g00, g10, g11, cross0, cross1 = lax.psum(parts, "row")
    upper0, inv0 = chol_inv(symmetric(g00))
    xmat = jnp.dot(g10, inv0.T, precision=highest, preferred_element_type=jnp.float32)
    schur = g11 - jnp.dot(xmat, xmat.T, precision=highest, preferred_element_type=jnp.float32)
    upper1, inv1 = chol_inv(symmetric(schur))
    proj0 = jnp.einsum("ab,bjt->ajt", inv0, cross0, precision=high)
    rest1 = cross1 - jnp.einsum("ab,bjt->ajt", xmat, proj0, precision=high)
    proj1 = jnp.einsum("ab,bjt->ajt", inv1, rest1, precision=high)
    basis0 = jnp.dot(panel0, inv0.T, precision=high, preferred_element_type=jnp.float32)
    resid1 = panel1 - jnp.dot(basis0, xmat.T, precision=high, preferred_element_type=jnp.float32)
    basis1 = jnp.dot(resid1, inv1.T, precision=high, preferred_element_type=jnp.float32)
    kept0 = jnp.where((glob > 0)[None, :, None], proj0, jnp.float32(0.0))
    kept1 = jnp.where((glob > 1)[None, :, None], proj1, jnp.float32(0.0))
    basis = jnp.concatenate([basis0, basis1], axis=1)
    kept = jnp.concatenate([kept0, kept1], axis=0)
    blocks = matrix - jnp.einsum("mb,bjt->mjt", basis, kept, precision=high)
    blocks = jnp.where((glob == 0)[None, :, None], basis0[:, None, :], blocks)
    blocks = jnp.where((glob == 1)[None, :, None], basis1[:, None, :], blocks)
    blocks = with_layout_constraint(blocks, Layout(major_to_minor=(0, 1, 2)))
    row0 = jnp.where((glob == 0)[None, :, None], upper0[:, None, :], kept0)
    row1 = jnp.where((glob == 1)[None, :, None], upper1[:, None, :], kept1)
    rows = with_layout_constraint(jnp.stack([row0, row1]), Layout(major_to_minor=(0, 1, 2, 3)))
    return (blocks, rows)


def solution(mesh):
    return jax.shard_map(
        shards,
        mesh=mesh,
        in_specs=(P("row", None, "col"),),
        out_specs=(P("row", None, "col"), P(None, None, None, "col")),
        check_vma=False,
    )
```

```python
import jax
import jax.numpy as jnp
from jax import lax
from jax.sharding import PartitionSpec as P
from jax.experimental.layout import Layout, with_layout_constraint
from jax.experimental import pallas as pl
from jax.experimental.pallas import tpu as pltpu

STEPS = 2

TILE = 128
GROUP = 8


def _mm(a, b):
    return jnp.dot(a, b, precision=lax.Precision.HIGHEST, preferred_element_type=jnp.float32)


def _factor(a, u_ref, m_ref, w_ref, t_ref, d_ref, e_ref):
    n = a.shape[0]
    nb = n // TILE
    w_ref[...] = a
    u_ref[...] = jnp.zeros_like(u_ref)
    m_ref[...] = jnp.zeros_like(m_ref)
    rows = lax.broadcasted_iota(jnp.int32, (TILE, TILE), 0)
    cols = lax.broadcasted_iota(jnp.int32, (TILE, TILE), 1)
    eye = jnp.where(rows == cols, 1.0, 0.0).astype(jnp.float32)
    sub = lax.broadcasted_iota(jnp.int32, (GROUP, 1), 0)
    lane = lax.broadcasted_iota(jnp.int32, (1, TILE), 1)
    rid = lax.broadcasted_iota(jnp.int32, (TILE, 1), 0)
    for b in range(nb):
        lo = b * TILE
        hi = lo + TILE
        t_ref[...] = w_ref[lo:hi, lo:hi]
        d_ref[...] = eye
        e_ref[...] = jnp.zeros_like(e_ref)

        def group(q, carry):
            base = pl.multiple_of(q * GROUP, GROUP)
            for r in range(GROUP):
                kk = q * GROUP + r
                a_row = t_ref[pl.ds(base, GROUP), :][r:r + 1, :]
                pivot = jnp.sum(jnp.where(lane == kk, a_row, 0.0), axis=1, keepdims=True)
                scale = 1.0 / jnp.sqrt(pivot)
                u = jnp.where(lane >= kk, a_row * scale, 0.0)
                u8 = e_ref[pl.ds(base, GROUP), :]
                e_ref[pl.ds(base, GROUP), :] = jnp.where(sub == r, u, u8)
                m8 = d_ref[pl.ds(base, GROUP), :]
                m_row = m8[r:r + 1, :] * scale
                d_ref[pl.ds(base, GROUP), :] = jnp.where(sub == r, m_row, m8)
                tile = t_ref[...]
                ucol = jnp.sum(jnp.where(cols == kk, tile, 0.0), axis=1, keepdims=True) * scale
                ucol = jnp.where(rid > kk, ucol, 0.0)
                t_ref[...] = tile - ucol * u
                d_ref[...] = d_ref[...] - ucol * m_row
            return carry

        lax.fori_loop(0, TILE // GROUP, group, 0)
        u_ref[lo:hi, lo:hi] = e_ref[...]
        m_ref[lo:hi, lo:hi] = d_ref[...]
        if b + 1 < nb:
            panel = _mm(d_ref[...], w_ref[lo:hi, hi:n])
            u_ref[lo:hi, hi:n] = panel
            w_ref[hi:n, hi:n] = w_ref[hi:n, hi:n] - _mm(panel.T, panel)
    for i in range(1, nb):
        di = m_ref[i * TILE:(i + 1) * TILE, i * TILE:(i + 1) * TILE]
        for j in range(i - 1, -1, -1):
            acc = jnp.zeros((TILE, TILE), jnp.float32)
            for k in range(j, i):
                low_ik = u_ref[k * TILE:(k + 1) * TILE, i * TILE:(i + 1) * TILE].T
                acc = acc + _mm(low_ik, m_ref[k * TILE:(k + 1) * TILE, j * TILE:(j + 1) * TILE])
            m_ref[i * TILE:(i + 1) * TILE, j * TILE:(j + 1) * TILE] = -_mm(di, acc)


def _pair_kernel(g00_ref, g10_ref, g11_ref, u0_ref, m0_ref, x_ref, u1_ref, m1_ref, w_ref, t_ref, d_ref, e_ref):
    g00 = g00_ref[...]
    _factor((g00 + g00.T) * 0.5, u0_ref, m0_ref, w_ref, t_ref, d_ref, e_ref)
    xmat = _mm(g10_ref[...], m0_ref[...].T)
    x_ref[...] = xmat
    schur = g11_ref[...] - _mm(xmat, xmat.T)
    _factor((schur + schur.T) * 0.5, u1_ref, m1_ref, w_ref, t_ref, d_ref, e_ref)


def factor_pair(g00, g10, g11):
    n = g00.shape[0]
    square = jax.ShapeDtypeStruct((n, n), jnp.float32)
    return pl.pallas_call(
        _pair_kernel,
        out_shape=(square,) * 5,
        scratch_shapes=[
            pltpu.VMEM((n, n), jnp.float32),
            pltpu.VMEM((TILE, TILE), jnp.float32),
            pltpu.VMEM((TILE, TILE), jnp.float32),
            pltpu.VMEM((TILE, TILE), jnp.float32),
        ],
        cost_estimate=pl.CostEstimate(flops=8 * n * n * n, bytes_accessed=8 * n * n * 4, transcendentals=2 * n),
    )(g00, g10, g11)


def shards(matrix):
    highest = lax.Precision.HIGHEST
    column = lax.axis_index("col")
    ncol = lax.axis_size("col")
    count = matrix.shape[1]
    width = matrix.shape[2]
    glob = jnp.arange(count, dtype=jnp.int32) * ncol + column
    own = matrix[:, 0, :]
    zero = jnp.zeros_like(own)
    panel0, panel1 = lax.psum(
        (jnp.where(column == 0, own, zero), jnp.where(column == 1, own, zero)), "col"
    )
    high = lax.Precision.HIGH
    parts = (
        jnp.dot(panel0.T, panel0, precision=highest, preferred_element_type=jnp.float32),
        jnp.dot(panel1.T, panel0, precision=highest, preferred_element_type=jnp.float32),
        jnp.dot(panel1.T, panel1, precision=highest, preferred_element_type=jnp.float32),
        jnp.einsum("mb,mjt->bjt", panel0, matrix, precision=high),
        jnp.einsum("mb,mjt->bjt", panel1, matrix, precision=high),
    )
    g00, g10, g11, cross0, cross1 = lax.psum(parts, "row")
    upper0, inv0, xmat, upper1, inv1 = factor_pair(g00, g10, g11)
    proj0 = jnp.einsum("ab,bjt->ajt", inv0, cross0, precision=high)
    rest1 = cross1 - jnp.einsum("ab,bjt->ajt", xmat, proj0, precision=high)
    proj1 = jnp.einsum("ab,bjt->ajt", inv1, rest1, precision=high)
    basis0 = jnp.dot(panel0, inv0.T, precision=high, preferred_element_type=jnp.float32)
    resid1 = panel1 - jnp.dot(basis0, xmat.T, precision=high, preferred_element_type=jnp.float32)
    basis1 = jnp.dot(resid1, inv1.T, precision=high, preferred_element_type=jnp.float32)
    kept0 = jnp.where((glob > 0)[None, :, None], proj0, jnp.float32(0.0))
    kept1 = jnp.where((glob > 1)[None, :, None], proj1, jnp.float32(0.0))
    basis = jnp.concatenate([basis0, basis1], axis=1)
    kept = jnp.concatenate([kept0, kept1], axis=0)
    blocks = matrix - jnp.einsum("mb,bjt->mjt", basis, kept, precision=high)
    blocks = jnp.where((glob == 0)[None, :, None], basis0[:, None, :], blocks)
    blocks = jnp.where((glob == 1)[None, :, None], basis1[:, None, :], blocks)
    blocks = with_layout_constraint(blocks, Layout(major_to_minor=(0, 1, 2)))
    row0 = jnp.where((glob == 0)[None, :, None], upper0[:, None, :], kept0)
    row1 = jnp.where((glob == 1)[None, :, None], upper1[:, None, :], kept1)
    rows = with_layout_constraint(jnp.stack([row0, row1]), Layout(major_to_minor=(0, 1, 2, 3)))
    return (blocks, rows)


def solution(mesh):
    return jax.shard_map(
        shards,
        mesh=mesh,
        in_specs=(P("row", None, "col"),),
        out_specs=(P("row", None, "col"), P(None, None, None, "col")),
        check_vma=False,
    )
```

```python
import jax
import jax.numpy as jnp
from jax import lax
from jax.sharding import PartitionSpec as P
from jax.experimental.layout import Layout, with_layout_constraint
from jax.experimental import pallas as pl
from jax.experimental.pallas import tpu as pltpu

STEPS = 2

TILE = 128
GROUP = 8


def _mm(a, b):
    return jnp.dot(a, b, precision=lax.Precision.HIGHEST, preferred_element_type=jnp.float32)


def _factor(a, u_ref, m_ref, w_ref, t_ref, d_ref, e_ref):
    n = a.shape[0]
    nb = n // TILE
    w_ref[...] = a
    u_ref[...] = jnp.zeros_like(u_ref)
    m_ref[...] = jnp.zeros_like(m_ref)
    rows = lax.broadcasted_iota(jnp.int32, (TILE, TILE), 0)
    cols = lax.broadcasted_iota(jnp.int32, (TILE, TILE), 1)
    eye = jnp.where(rows == cols, 1.0, 0.0).astype(jnp.float32)
    sub = lax.broadcasted_iota(jnp.int32, (GROUP, 1), 0)
    lane = lax.broadcasted_iota(jnp.int32, (1, TILE), 1)
    rid = lax.broadcasted_iota(jnp.int32, (TILE, 1), 0)
    for b in range(nb):
        lo = b * TILE
        hi = lo + TILE
        t_ref[...] = w_ref[lo:hi, lo:hi]
        d_ref[...] = eye
        e_ref[...] = jnp.zeros_like(e_ref)

        def group(q, carry):
            base = pl.multiple_of(q * GROUP, GROUP)
            for r in range(GROUP):
                kk = q * GROUP + r
                a_row = t_ref[pl.ds(base, GROUP), :][r:r + 1, :]
                pivot = jnp.sum(jnp.where(lane == kk, a_row, 0.0), axis=1, keepdims=True)
                scale = 1.0 / jnp.sqrt(pivot)
                u = jnp.where(lane >= kk, a_row * scale, 0.0)
                u8 = e_ref[pl.ds(base, GROUP), :]
                e_ref[pl.ds(base, GROUP), :] = jnp.where(sub == r, u, u8)
                m8 = d_ref[pl.ds(base, GROUP), :]
                m_row = m8[r:r + 1, :] * scale
                d_ref[pl.ds(base, GROUP), :] = jnp.where(sub == r, m_row, m8)
                tile = t_ref[...]
                ucol = jnp.sum(jnp.where(cols == kk, tile, 0.0), axis=1, keepdims=True) * scale
                ucol = jnp.where(rid > kk, ucol, 0.0)
                t_ref[...] = tile - ucol * u
                d_ref[...] = d_ref[...] - ucol * m_row
            return carry

        lax.fori_loop(0, TILE // GROUP, group, 0)
        u_ref[lo:hi, lo:hi] = e_ref[...]
        m_ref[lo:hi, lo:hi] = d_ref[...]
        if b + 1 < nb:
            panel = _mm(d_ref[...], w_ref[lo:hi, hi:n])
            u_ref[lo:hi, hi:n] = panel
            w_ref[hi:n, hi:n] = w_ref[hi:n, hi:n] - _mm(panel.T, panel)
    for i in range(1, nb):
        di = m_ref[i * TILE:(i + 1) * TILE, i * TILE:(i + 1) * TILE]
        for j in range(i - 1, -1, -1):
            acc = jnp.zeros((TILE, TILE), jnp.float32)
            for k in range(j, i):
                low_ik = u_ref[k * TILE:(k + 1) * TILE, i * TILE:(i + 1) * TILE].T
                acc = acc + _mm(low_ik, m_ref[k * TILE:(k + 1) * TILE, j * TILE:(j + 1) * TILE])
            m_ref[i * TILE:(i + 1) * TILE, j * TILE:(j + 1) * TILE] = -_mm(di, acc)


def _pair_kernel(g00_ref, g10_ref, g11_ref, u0_ref, m0_ref, x_ref, u1_ref, m1_ref, w_ref, t_ref, d_ref, e_ref):
    g00 = g00_ref[...]
    _factor((g00 + g00.T) * 0.5, u0_ref, m0_ref, w_ref, t_ref, d_ref, e_ref)
    xmat = _mm(g10_ref[...], m0_ref[...].T)
    x_ref[...] = xmat
    schur = g11_ref[...] - _mm(xmat, xmat.T)
    _factor((schur + schur.T) * 0.5, u1_ref, m1_ref, w_ref, t_ref, d_ref, e_ref)


def factor_pair(g00, g10, g11):
    n = g00.shape[0]
    square = jax.ShapeDtypeStruct((n, n), jnp.float32)
    return pl.pallas_call(
        _pair_kernel,
        out_shape=(square,) * 5,
        scratch_shapes=[
            pltpu.VMEM((n, n), jnp.float32),
            pltpu.VMEM((TILE, TILE), jnp.float32),
            pltpu.VMEM((TILE, TILE), jnp.float32),
            pltpu.VMEM((TILE, TILE), jnp.float32),
        ],
        cost_estimate=pl.CostEstimate(flops=8 * n * n * n, bytes_accessed=8 * n * n * 4, transcendentals=2 * n),
    )(g00, g10, g11)


def shards(matrix):
    highest = lax.Precision.HIGHEST
    column = lax.axis_index("col")
    ncol = lax.axis_size("col")
    count = matrix.shape[1]
    width = matrix.shape[2]
    glob = jnp.arange(count, dtype=jnp.int32) * ncol + column
    own = with_layout_constraint(matrix, Layout(major_to_minor=(0, 1, 2)))[:, 0, :]
    zero = jnp.zeros_like(own)
    panel0, panel1 = lax.psum(
        (jnp.where(column == 0, own, zero), jnp.where(column == 1, own, zero)), "col"
    )
    high = lax.Precision.HIGH
    parts = (
        jnp.dot(panel0.T, panel0, precision=highest, preferred_element_type=jnp.float32),
        jnp.dot(panel1.T, panel0, precision=highest, preferred_element_type=jnp.float32),
        jnp.dot(panel1.T, panel1, precision=highest, preferred_element_type=jnp.float32),
        jnp.einsum("mb,mjt->bjt", panel0, matrix, precision=high),
        jnp.einsum("mb,mjt->bjt", panel1, matrix, precision=high),
    )
    g00, g10, g11, cross0, cross1 = lax.psum(parts, "row")
    upper0, inv0, xmat, upper1, inv1 = factor_pair(g00, g10, g11)
    proj0 = jnp.einsum("ab,bjt->ajt", inv0, cross0, precision=high)
    rest1 = cross1 - jnp.einsum("ab,bjt->ajt", xmat, proj0, precision=high)
    proj1 = jnp.einsum("ab,bjt->ajt", inv1, rest1, precision=high)
    basis0 = jnp.dot(panel0, inv0.T, precision=high, preferred_element_type=jnp.float32)
    resid1 = panel1 - jnp.dot(basis0, xmat.T, precision=high, preferred_element_type=jnp.float32)
    basis1 = jnp.dot(resid1, inv1.T, precision=high, preferred_element_type=jnp.float32)
    kept0 = jnp.where((glob > 0)[None, :, None], proj0, jnp.float32(0.0))
    kept1 = jnp.where((glob > 1)[None, :, None], proj1, jnp.float32(0.0))
    basis = jnp.concatenate([basis0, basis1], axis=1)
    kept = jnp.concatenate([kept0, kept1], axis=0)
    blocks = matrix - jnp.einsum("mb,bjt->mjt", basis, kept, precision=high)
    blocks = jnp.where((glob == 0)[None, :, None], basis0[:, None, :], blocks)
    blocks = jnp.where((glob == 1)[None, :, None], basis1[:, None, :], blocks)
    blocks = with_layout_constraint(blocks, Layout(major_to_minor=(0, 1, 2)))
    row0 = jnp.where((glob == 0)[None, :, None], upper0[:, None, :], kept0)
    row1 = jnp.where((glob == 1)[None, :, None], upper1[:, None, :], kept1)
    rows = with_layout_constraint(jnp.stack([row0, row1]), Layout(major_to_minor=(0, 1, 2, 3)))
    return (blocks, rows)


def solution(mesh):
    return jax.shard_map(
        shards,
        mesh=mesh,
        in_specs=(P("row", None, "col"),),
        out_specs=(P("row", None, "col"), P(None, None, None, "col")),
        check_vma=False,
    )
```

```python
import jax
import jax.numpy as jnp
from jax import lax
from jax.sharding import PartitionSpec as P
from jax.experimental.layout import Layout, with_layout_constraint
from jax.experimental import pallas as pl
from jax.experimental.pallas import tpu as pltpu

STEPS = 2

TILE = 128
GROUP = 8


def _mm(a, b):
    return jnp.dot(a, b, precision=lax.Precision.HIGHEST, preferred_element_type=jnp.float32)


def _factor(a, u_ref, m_ref, w_ref, t_ref, d_ref, e_ref):
    n = a.shape[0]
    nb = n // TILE
    w_ref[...] = a
    u_ref[...] = jnp.zeros_like(u_ref)
    m_ref[...] = jnp.zeros_like(m_ref)
    rows = lax.broadcasted_iota(jnp.int32, (TILE, TILE), 0)
    cols = lax.broadcasted_iota(jnp.int32, (TILE, TILE), 1)
    eye = jnp.where(rows == cols, 1.0, 0.0).astype(jnp.float32)
    sub = lax.broadcasted_iota(jnp.int32, (GROUP, 1), 0)
    lane = lax.broadcasted_iota(jnp.int32, (1, TILE), 1)
    rid = lax.broadcasted_iota(jnp.int32, (TILE, 1), 0)
    for b in range(nb):
        lo = b * TILE
        hi = lo + TILE
        t_ref[...] = w_ref[lo:hi, lo:hi]
        d_ref[...] = eye
        e_ref[...] = jnp.zeros_like(e_ref)

        def group(q, carry):
            base = pl.multiple_of(q * GROUP, GROUP)
            for r in range(GROUP):
                kk = q * GROUP + r
                a_row = t_ref[pl.ds(base, GROUP), :][r:r + 1, :]
                pivot = jnp.sum(jnp.where(lane == kk, a_row, 0.0), axis=1, keepdims=True)
                scale = 1.0 / jnp.sqrt(pivot)
                u = jnp.where(lane >= kk, a_row * scale, 0.0)
                u8 = e_ref[pl.ds(base, GROUP), :]
                e_ref[pl.ds(base, GROUP), :] = jnp.where(sub == r, u, u8)
                m8 = d_ref[pl.ds(base, GROUP), :]
                m_row = m8[r:r + 1, :] * scale
                d_ref[pl.ds(base, GROUP), :] = jnp.where(sub == r, m_row, m8)
                tile = t_ref[...]
                ucol = jnp.sum(jnp.where(cols == kk, tile, 0.0), axis=1, keepdims=True) * scale
                ucol = jnp.where(rid > kk, ucol, 0.0)
                t_ref[...] = tile - ucol * u
                d_ref[...] = d_ref[...] - ucol * m_row
            return carry

        lax.fori_loop(0, TILE // GROUP, group, 0)
        u_ref[lo:hi, lo:hi] = e_ref[...]
        m_ref[lo:hi, lo:hi] = d_ref[...]
        if b + 1 < nb:
            panel = _mm(d_ref[...], w_ref[lo:hi, hi:n])
            u_ref[lo:hi, hi:n] = panel
            w_ref[hi:n, hi:n] = w_ref[hi:n, hi:n] - _mm(panel.T, panel)
    for i in range(1, nb):
        di = m_ref[i * TILE:(i + 1) * TILE, i * TILE:(i + 1) * TILE]
        for j in range(i - 1, -1, -1):
            acc = jnp.zeros((TILE, TILE), jnp.float32)
            for k in range(j, i):
                low_ik = u_ref[k * TILE:(k + 1) * TILE, i * TILE:(i + 1) * TILE].T
                acc = acc + _mm(low_ik, m_ref[k * TILE:(k + 1) * TILE, j * TILE:(j + 1) * TILE])
            m_ref[i * TILE:(i + 1) * TILE, j * TILE:(j + 1) * TILE] = -_mm(di, acc)


def _pair_kernel(g00_ref, g10_ref, g11_ref, u0_ref, m0_ref, x_ref, u1_ref, m1_ref, w_ref, t_ref, d_ref, e_ref):
    g00 = g00_ref[...]
    _factor((g00 + g00.T) * 0.5, u0_ref, m0_ref, w_ref, t_ref, d_ref, e_ref)
    xmat = _mm(g10_ref[...], m0_ref[...].T)
    x_ref[...] = xmat
    schur = g11_ref[...] - _mm(xmat, xmat.T)
    _factor((schur + schur.T) * 0.5, u1_ref, m1_ref, w_ref, t_ref, d_ref, e_ref)


def factor_pair(g00, g10, g11):
    n = g00.shape[0]
    square = jax.ShapeDtypeStruct((n, n), jnp.float32)
    return pl.pallas_call(
        _pair_kernel,
        out_shape=(square,) * 5,
        scratch_shapes=[
            pltpu.VMEM((n, n), jnp.float32),
            pltpu.VMEM((TILE, TILE), jnp.float32),
            pltpu.VMEM((TILE, TILE), jnp.float32),
            pltpu.VMEM((TILE, TILE), jnp.float32),
        ],
        cost_estimate=pl.CostEstimate(flops=8 * n * n * n, bytes_accessed=8 * n * n * 4, transcendentals=2 * n),
    )(g00, g10, g11)


def shards(matrix):
    highest = lax.Precision.HIGHEST
    column = lax.axis_index("col")
    ncol = lax.axis_size("col")
    count = matrix.shape[1]
    width = matrix.shape[2]
    glob = jnp.arange(count, dtype=jnp.int32) * ncol + column
    own = matrix[:, 0, :]
    zero = jnp.zeros_like(own)
    panel0, panel1 = lax.psum(
        (jnp.where(column == 0, own, zero), jnp.where(column == 1, own, zero)), "col"
    )
    high = lax.Precision.HIGH
    both = jnp.concatenate([panel0, panel1], axis=1)
    parts = (
        jnp.dot(both.T, both, precision=highest, preferred_element_type=jnp.float32),
        jnp.einsum("mb,mjt->bjt", both, matrix, precision=high),
    )
    gram, cross = lax.psum(parts, "row")
    g00 = gram[:width, :width]
    g10 = gram[width:, :width]
    g11 = gram[width:, width:]
    cross0 = cross[:width]
    cross1 = cross[width:]
    upper0, inv0, xmat, upper1, inv1 = factor_pair(g00, g10, g11)
    proj0 = jnp.einsum("ab,bjt->ajt", inv0, cross0, precision=high)
    rest1 = cross1 - jnp.einsum("ab,bjt->ajt", xmat, proj0, precision=high)
    proj1 = jnp.einsum("ab,bjt->ajt", inv1, rest1, precision=high)
    basis0 = jnp.dot(panel0, inv0.T, precision=high, preferred_element_type=jnp.float32)
    resid1 = panel1 - jnp.dot(basis0, xmat.T, precision=high, preferred_element_type=jnp.float32)
    basis1 = jnp.dot(resid1, inv1.T, precision=high, preferred_element_type=jnp.float32)
    kept0 = jnp.where((glob > 0)[None, :, None], proj0, jnp.float32(0.0))
    kept1 = jnp.where((glob > 1)[None, :, None], proj1, jnp.float32(0.0))
    basis = jnp.concatenate([basis0, basis1], axis=1)
    kept = jnp.concatenate([kept0, kept1], axis=0)
    blocks = matrix - jnp.einsum("mb,bjt->mjt", basis, kept, precision=high)
    blocks = jnp.where((glob == 0)[None, :, None], basis0[:, None, :], blocks)
    blocks = jnp.where((glob == 1)[None, :, None], basis1[:, None, :], blocks)
    blocks = with_layout_constraint(blocks, Layout(major_to_minor=(0, 1, 2)))
    row0 = jnp.where((glob == 0)[None, :, None], upper0[:, None, :], kept0)
    row1 = jnp.where((glob == 1)[None, :, None], upper1[:, None, :], kept1)
    rows = with_layout_constraint(jnp.stack([row0, row1]), Layout(major_to_minor=(0, 1, 2, 3)))
    return (blocks, rows)


def solution(mesh):
    return jax.shard_map(
        shards,
        mesh=mesh,
        in_specs=(P("row", None, "col"),),
        out_specs=(P("row", None, "col"), P(None, None, None, "col")),
        check_vma=False,
    )
```
